32 devices in a mesh: seq: 16 (over z, y, core), batch: 2 (over x).
Axes of the slice: x: 2, y: 2, z: 4, core: 2. Of those that a mesh axis runs over, the one named last changes fastest.
Arguments:
- block_input: bfloat16 [4, 1536, 2048], P('batch', None, 'seq'), may hold values from -6 to 6
- tap_weight: bfloat16 [9, 1536], replicated, may hold values from -2 to 2
- mix_weight: bfloat16 [1536, 1536], replicated, may hold values from -0.15625 to 0.15625
- head_grad: bfloat16 [4, 1536, 2048], P('batch', 'seq'), may hold values from -6 to 6
Outputs:
- block_output: bfloat16 [4, 1536, 2048], P('batch', None, 'seq')
- d_input: bfloat16 [4, 1536, 2048], P('batch', None, 'seq')
- tap_grad: float32 [9, 1536], replicated
- mix_grad: float32 [1536, 1536], P('seq')
The draws below stay inside these ranges and needn't reach their ends.
All inputs are finite; a program needn't handle non-finite values.
Results may differ from the reference program's by a relative error of at most 0.005.
Values may be sent and summed in bfloat16 or wider, within the bound.
No kernel may reach another device: no remote copies, remote signals or barrier semaphores. Data moves between devices by JAX's collectives and lax.ppermute only.
A program may use at most 128 MiB of HBM per device.

```python
import math
import jax
import jax.numpy as jnp
from jax import lax

C = 1536
K = 9
SEQS = 4
TOKENS = 2048
DILATION_STEP = 512


def raised(drawn, key, source, target, blocks, factor):
    def block_of(axis_at):
        return (jnp.arange(drawn.shape[axis_at]) // (drawn.shape[axis_at] // blocks)).reshape((-1,) + (1,) * (drawn.ndim - 1 - axis_at))

    one_side = jax.random.permutation(key, blocks)[block_of(target)]
    other_side = (block_of(target) + blocks // 2) % blocks
    return jnp.where((block_of(source) == one_side) | (block_of(source) == other_side), factor * drawn, drawn)


def shard_levels(key, extent, split, least, top_value):
    loudness = 1.0
    for axis_at, shards_of in split:
        steps = jax.random.uniform(jax.random.fold_in(jax.random.fold_in(key, 6), axis_at), (shards_of,), jnp.float32, least / len(split), top_value / len(split))
        loudness = loudness * jnp.repeat(jnp.exp(steps), extent[axis_at] // shards_of).reshape((-1,) + (1,) * (len(extent) - 1 - axis_at))
    return loudness


def centred(key, dims, width, most, pieces=(), held_as=jnp.bfloat16):
    loudness = shard_levels(key, dims, pieces, -0.22, 0.18) if pieces else 1.0
    drawn = jax.random.normal(key, dims, jnp.float32) * width * loudness
    return jnp.minimum(jnp.maximum(drawn, -most), most).astype(held_as)


def heavy_noise(own_key, dims, spread, limit, shards, heavy, held_as=jnp.bfloat16):
    values = spread * jax.random.normal(own_key, dims, jnp.float32)
    if shards:
        values = values * shard_levels(own_key, dims, shards, -0.22, 0.18)
    return jnp.clip(raised(values, jax.random.fold_in(own_key, 3), *heavy), -limit, limit).astype(held_as)


def setup_inputs(seed: int = 0) -> dict:
    keys = jax.random.split(jax.random.key(seed), 5)
    block_input = heavy_noise(keys[0], (SEQS, C, TOKENS), 1.0, 6.0, ((0, 2), (2, 16)), (2, 1, 16, 2.0))
    tap_weight = centred(keys[1], (K, C), K ** -0.5, 2.0)
    mix_weight = centred(keys[2], (C, C), C ** -0.5, 0.15625)
    head_grad = centred(keys[3], (SEQS, C, TOKENS), 1.0, 6.0, ((0, 2), (1, 16)))
    return {"block_input": block_input, "tap_weight": tap_weight, "mix_weight": mix_weight, "head_grad": head_grad}


def gelu_parts(values):
    normal_cdf = 0.5 * (1.0 + jax.scipy.special.erf(values / math.sqrt(2.0)))
    normal_pdf = jnp.exp(-0.5 * values * values) / math.sqrt(2.0 * math.pi)
    return (values * normal_cdf, normal_cdf + values * normal_pdf)

def shifted(receptive_span, tap_offset):
    padded_input = jnp.pad(receptive_span, ((0, 0), (4 * DILATION_STEP, 4 * DILATION_STEP)))
    window_begin = 4 * DILATION_STEP + tap_offset * DILATION_STEP
    return lax.slice_in_dim(padded_input, window_begin, window_begin + TOKENS, axis=1)

def reference(block_input, tap_weight, mix_weight, head_grad):
    kernel = tap_weight.astype(jnp.float32)
    mixing = mix_weight.astype(jnp.float32)
    largest_offset = lax.Precision.HIGHEST
    outputs = []
    gradients = []
    tap_total = jnp.zeros((K, C), jnp.float32)
    mix_total = jnp.zeros((C, C), jnp.float32)
    for seq_index in range(SEQS):
        receptive_span = block_input[seq_index].astype(jnp.float32)
        views = [shifted(receptive_span, k - 4) for k in range(K)]
        before_gelu = jnp.zeros((C, TOKENS), jnp.float32)
        for k in range(K):
            before_gelu = before_gelu + kernel[k][:, None] * views[k]
        activated, slope = gelu_parts(before_gelu)
        gated = activated.astype(jnp.bfloat16).astype(jnp.float32)
        mixed = jnp.einsum('co,ct->ot', mixing, gated, precision=largest_offset)
        outputs.append((receptive_span + mixed).astype(jnp.bfloat16))
        upper = head_grad[seq_index].astype(jnp.float32)
        backward = jnp.einsum('co,ot->ct', mixing, upper, precision=largest_offset)
        grad_pre = (backward * slope).astype(jnp.bfloat16).astype(jnp.float32)
        result = upper
        for k in range(K):
            result = result + kernel[k][:, None] * shifted(grad_pre, 4 - k)
        gradients.append(result.astype(jnp.bfloat16))
        tap_total = tap_total + jnp.stack([lax.optimization_barrier(jnp.sum(grad_pre * views[k], axis=1)) for k in range(K)])
        mix_total = mix_total + jnp.einsum('ct,ot->co', gated, upper, precision=largest_offset)
    return (jnp.stack(outputs), jnp.stack(gradients), tap_total, mix_total)
```

```python
import math

import jax
import jax.numpy as jnp
from jax import lax
from jax.sharding import PartitionSpec as P

DILATION_STEP = 512
TAPS = 9


def gelu_parts(values):
    normal_cdf = 0.5 * (1.0 + jax.scipy.special.erf(values / math.sqrt(2.0)))
    normal_pdf = jnp.exp(-0.5 * values * values) / math.sqrt(2.0 * math.pi)
    return (values * normal_cdf, normal_cdf + values * normal_pdf)


def shifted(field, tap_offset):
    tokens = field.shape[-1]
    by = tap_offset * DILATION_STEP
    if abs(by) >= tokens:
        return jnp.zeros_like(field)
    pad = [(0, 0)] * (field.ndim - 1)
    if by > 0:
        return jnp.pad(field[..., by:], pad + [(0, by)])
    if by < 0:
        return jnp.pad(field[..., :by], pad + [(-by, 0)])
    return field


def to_channels(x):
    return lax.all_to_all(x, "seq", split_axis=1, concat_axis=2, tiled=True)


def to_positions(x):
    return lax.all_to_all(x, "seq", split_axis=2, concat_axis=1, tiled=True)


def body(block_input, tap_weight, mix_weight, head_grad):
    n_seq = lax.axis_size("seq")
    channels = block_input.shape[1]
    local_channels = channels // n_seq
    me = lax.axis_index("seq")
    kernel = lax.dynamic_slice_in_dim(tap_weight, me * local_channels, local_channels, axis=1).astype(jnp.float32)

    x_c = to_channels(block_input).astype(jnp.float32)
    before_gelu = jnp.zeros(x_c.shape, jnp.float32)
    for k in range(TAPS):
        before_gelu = before_gelu + kernel[k][None, :, None] * shifted(x_c, k - 4)
    activated, slope = gelu_parts(before_gelu)
    gated_c = activated.astype(jnp.bfloat16)

    gated = to_positions(gated_c)
    mixed = jnp.einsum("co,sct->sot", mix_weight, gated, preferred_element_type=jnp.float32)
    block_output = (block_input.astype(jnp.float32) + mixed).astype(jnp.bfloat16)

    upper = to_positions(head_grad)
    backward = jnp.einsum("co,sot->sct", mix_weight, upper, preferred_element_type=jnp.float32)
    backward_c = to_channels(backward)
    grad_pre = (backward_c * slope).astype(jnp.bfloat16).astype(jnp.float32)

    result = head_grad.astype(jnp.float32)
    for k in range(TAPS):
        result = result + kernel[k][None, :, None] * shifted(grad_pre, 4 - k)
    d_input = to_positions(result.astype(jnp.bfloat16))

    local_taps = jnp.stack([jnp.sum(grad_pre * shifted(x_c, k - 4), axis=(0, 2)) for k in range(TAPS)])
    tap_grad = lax.all_gather(lax.psum(local_taps, "batch"), "seq", axis=1, tiled=True)

    partial_rows = lax.psum_scatter(
        jnp.einsum("sct,sot->co", gated, upper, preferred_element_type=jnp.float32),
        ("seq", "batch"),
        scatter_dimension=0,
        tiled=True,
    )
    mix_grad = lax.all_gather(partial_rows, "batch", axis=0, tiled=True)
    return (block_output, d_input, tap_grad, mix_grad)


def solution(mesh):
    placed = (P("batch", None, "seq"), P(), P(), P("batch", "seq", None))
    return jax.shard_map(
        body,
        mesh=mesh,
        in_specs=placed,
        out_specs=(P("batch", None, "seq"), P("batch", None, "seq"), P(), P("seq", None)),
        check_vma=False,
    )
```

```python
import math

import jax
import jax.numpy as jnp
from jax import lax
from jax.sharding import PartitionSpec as P

DILATION_STEP = 512
TAPS = 9


def gelu_parts(values):
    normal_cdf = 0.5 * (1.0 + jax.scipy.special.erf(values / math.sqrt(2.0)))
    normal_pdf = jnp.exp(-0.5 * values * values) / math.sqrt(2.0 * math.pi)
    return (values * normal_cdf, normal_cdf + values * normal_pdf)


def shifted(field, tap_offset):
    tokens = field.shape[-1]
    by = tap_offset * DILATION_STEP
    if abs(by) >= tokens:
        return jnp.zeros_like(field)
    pad = [(0, 0)] * (field.ndim - 1)
    if by > 0:
        return jnp.pad(field[..., by:], pad + [(0, by)])
    if by < 0:
        return jnp.pad(field[..., :by], pad + [(-by, 0)])
    return field


def to_channels(x):
    return lax.all_to_all(x, "seq", split_axis=1, concat_axis=2, tiled=True)


def to_positions(x):
    return lax.all_to_all(x, "seq", split_axis=2, concat_axis=1, tiled=True)


def body(block_input, tap_weight, mix_weight, head_grad):
    n_seq = lax.axis_size("seq")
    channels = block_input.shape[1]
    local_channels = channels // n_seq
    me = lax.axis_index("seq")
    kernel = lax.dynamic_slice_in_dim(tap_weight, me * local_channels, local_channels, axis=1).astype(jnp.float32)

    x_c = to_channels(block_input).astype(jnp.float32)
    before_gelu = jnp.zeros(x_c.shape, jnp.float32)
    for k in range(TAPS):
        before_gelu = before_gelu + kernel[k][None, :, None] * shifted(x_c, k - 4)
    activated, slope = gelu_parts(before_gelu)
    gated_c = activated.astype(jnp.bfloat16)

    gated = to_positions(gated_c)
    mixed = jnp.einsum("co,sct->sot", mix_weight, gated, preferred_element_type=jnp.float32)
    block_output = (block_input.astype(jnp.float32) + mixed).astype(jnp.bfloat16)

    upper = to_positions(head_grad)
    backward = jnp.einsum("co,sot->sct", mix_weight, upper, preferred_element_type=jnp.float32)
    backward_c = to_channels(backward.astype(jnp.bfloat16)).astype(jnp.float32)
    grad_pre = (backward_c * slope).astype(jnp.bfloat16).astype(jnp.float32)

    result = head_grad.astype(jnp.float32)
    for k in range(TAPS):
        result = result + kernel[k][None, :, None] * shifted(grad_pre, 4 - k)
    d_input = to_positions(result.astype(jnp.bfloat16))

    local_taps = jnp.stack([jnp.sum(grad_pre * shifted(x_c, k - 4), axis=(0, 2)) for k in range(TAPS)])
    tap_grad = lax.all_gather(lax.psum(local_taps, "batch"), "seq", axis=1, tiled=True)

    n_batch = lax.axis_size("batch")
    rows_per = channels // n_seq
    part = rows_per // n_batch
    both_gated = lax.all_gather(gated, "batch", axis=0, tiled=True)
    both_upper = lax.all_gather(upper, "batch", axis=0, tiled=True)
    seqs = both_gated.shape[0]
    picked = both_gated.reshape(seqs, n_seq, n_batch, part, both_gated.shape[-1])
    picked = lax.dynamic_index_in_dim(picked, lax.axis_index("batch"), axis=2, keepdims=False)
    picked = picked.reshape(seqs, n_seq * part, both_gated.shape[-1])
    partial_rows = lax.psum_scatter(
        jnp.einsum("sct,sot->co", picked, both_upper, preferred_element_type=jnp.float32),
        "seq",
        scatter_dimension=0,
        tiled=True,
    )
    mix_grad = lax.all_gather(partial_rows, "batch", axis=0, tiled=True)
    return (block_output, d_input, tap_grad, mix_grad)


def solution(mesh):
    placed = (P("batch", None, "seq"), P(), P(), P("batch", "seq", None))
    return jax.shard_map(
        body,
        mesh=mesh,
        in_specs=placed,
        out_specs=(P("batch", None, "seq"), P("batch", None, "seq"), P(), P("seq", None)),
        check_vma=False,
    )
```

```python
import math

import jax
import jax.numpy as jnp
from jax import lax
from jax.sharding import PartitionSpec as P

DILATION_STEP = 512
TAPS = 9


def gelu_parts(values):
    normal_cdf = 0.5 * (1.0 + jax.scipy.special.erf(values / math.sqrt(2.0)))
    normal_pdf = jnp.exp(-0.5 * values * values) / math.sqrt(2.0 * math.pi)
    return (values * normal_cdf, normal_cdf + values * normal_pdf)


def shifted_blocks(field, by):
    blocks = field.shape[0]
    if abs(by) >= blocks:
        return jnp.zeros_like(field)
    pad = [(0, 0)] * (field.ndim - 1)
    if by > 0:
        return jnp.pad(field[by:], [(0, by)] + pad)
    if by < 0:
        return jnp.pad(field[:by], [(-by, 0)] + pad)
    return field


def exchange(blocks):
    return lax.all_to_all(blocks, "seq", split_axis=0, concat_axis=0, tiled=True)


def by_channel_block(field, n):
    s, c, t = field.shape
    return field.reshape(s, n, c // n, t).transpose(1, 0, 2, 3)


def from_channel_blocks(blocks):
    n, s, cl, t = blocks.shape
    return blocks.transpose(1, 0, 2, 3).reshape(s, n * cl, t)


def xor_gather(piece, axis, count):
    me = lax.axis_index(axis)
    held = piece[None]
    step = 1
    while step < count:
        received = lax.ppermute(held, axis, [(d, d ^ step) for d in range(count)])
        low = ((me // step) % 2) == 0
        held = jnp.where(low, jnp.concatenate([held, received]), jnp.concatenate([received, held]))
        step *= 2
    return held


def xor_sum(piece, axis, count):
    step = 1
    while step < count:
        piece = piece + lax.ppermute(piece, axis, [(d, d ^ step) for d in range(count)])
        step *= 2
    return piece


def body(block_input, tap_weight, mix_weight, head_grad):
    n_seq = lax.axis_size("seq")
    n_batch = lax.axis_size("batch")
    seqs, channels, t_local = block_input.shape
    local_channels = channels // n_seq
    hop = DILATION_STEP // t_local
    me = lax.axis_index("seq")
    kernel = lax.dynamic_slice_in_dim(tap_weight, me * local_channels, local_channels, axis=1).astype(jnp.float32)

    dy_blocks = head_grad.reshape(seqs, local_channels, n_seq, t_local).transpose(2, 0, 1, 3)

    first = exchange(jnp.stack([by_channel_block(block_input, n_seq), dy_blocks], axis=1))
    x_c = first[:, 0].astype(jnp.float32)
    upper = from_channel_blocks(first[:, 1])

    before_gelu = jnp.zeros(x_c.shape, jnp.float32)
    for k in range(TAPS):
        before_gelu = before_gelu + kernel[k][None, None, :, None] * shifted_blocks(x_c, (k - 4) * hop)
    activated, slope = gelu_parts(before_gelu)
    gated_c = activated.astype(jnp.bfloat16)

    backward = jnp.einsum("co,sot->sct", mix_weight, upper, preferred_element_type=jnp.float32)

    second = exchange(jnp.stack([gated_c, by_channel_block(backward.astype(jnp.bfloat16), n_seq)], axis=1))
    gated = from_channel_blocks(second[:, 0])
    backward_c = second[:, 1].astype(jnp.float32)

    mixed = jnp.einsum("co,sct->sot", mix_weight, gated, preferred_element_type=jnp.float32)
    block_output = (block_input.astype(jnp.float32) + mixed).astype(jnp.bfloat16)

    grad_pre = (backward_c * slope).astype(jnp.bfloat16).astype(jnp.float32)
    result = dy_blocks.astype(jnp.float32)
    for k in range(TAPS):
        result = result + kernel[k][None, None, :, None] * shifted_blocks(grad_pre, (4 - k) * hop)
    d_input = from_channel_blocks(exchange(result.astype(jnp.bfloat16)))

    local_taps = jnp.stack(
        [jnp.sum(grad_pre * shifted_blocks(x_c, (k - 4) * hop), axis=(0, 1, 3)) for k in range(TAPS)]
    )
    taps_all = xor_gather(xor_sum(local_taps, "batch", n_batch), "seq", n_seq)
    tap_grad = taps_all.transpose(1, 0, 2).reshape(TAPS, channels)

    part = local_channels // n_batch
    both_gated = lax.all_gather(gated, "batch", axis=0, tiled=True)
    both_upper = lax.all_gather(upper, "batch", axis=0, tiled=True)
    all_seqs = both_gated.shape[0]
    picked = both_gated.reshape(all_seqs, n_seq, n_batch, part, t_local)
    picked = lax.dynamic_index_in_dim(picked, lax.axis_index("batch"), axis=2, keepdims=False)
    picked = picked.reshape(all_seqs, n_seq * part, t_local)
    partial_rows = lax.psum_scatter(
        jnp.einsum("sct,sot->co", picked, both_upper, preferred_element_type=jnp.float32),
        "seq",
        scatter_dimension=0,
        tiled=True,
    )
    mix_grad = lax.all_gather(partial_rows, "batch", axis=0, tiled=True)
    return (block_output, d_input, tap_grad, mix_grad)


def solution(mesh):
    placed = (P("batch", None, "seq"), P(), P(), P("batch", "seq", None))
    return jax.shard_map(
        body,
        mesh=mesh,
        in_specs=placed,
        out_specs=(P("batch", None, "seq"), P("batch", None, "seq"), P(), P("seq", None)),
        check_vma=False,
    )
```

```python
import math

import jax
import jax.numpy as jnp
from jax import lax
from jax.sharding import PartitionSpec as P

DILATION_STEP = 512
TAPS = 9


def gelu_parts(values):
    normal_cdf = 0.5 * (1.0 + jax.scipy.special.erf(values / math.sqrt(2.0)))
    normal_pdf = jnp.exp(-0.5 * values * values) / math.sqrt(2.0 * math.pi)
    return (values * normal_cdf, normal_cdf + values * normal_pdf)


def shifted_blocks(field, by):
    blocks = field.shape[0]
    if abs(by) >= blocks:
        return jnp.zeros_like(field)
    pad = [(0, 0)] * (field.ndim - 1)
    if by > 0:
        return jnp.pad(field[by:], [(0, by)] + pad)
    if by < 0:
        return jnp.pad(field[:by], [(-by, 0)] + pad)
    return field


def exchange(blocks):
    return lax.all_to_all(blocks, "seq", split_axis=0, concat_axis=0, tiled=True)


def by_channel_block(field, n):
    s, c, t = field.shape
    return field.reshape(s, n, c // n, t).transpose(1, 0, 2, 3)


def from_channel_blocks(blocks):
    n, s, cl, t = blocks.shape
    return blocks.transpose(1, 0, 2, 3).reshape(s, n * cl, t)


def xor_gather(piece, axis, count):
    me = lax.axis_index(axis)
    held = piece[None]
    step = 1
    while step < count:
        received = lax.ppermute(held, axis, [(d, d ^ step) for d in range(count)])
        low = ((me // step) % 2) == 0
        held = jnp.where(low, jnp.concatenate([held, received]), jnp.concatenate([received, held]))
        step *= 2
    return held


def ring_shift(piece, axis, count, by):
    return lax.ppermute(piece, axis, [(d, (d + by) % count) for d in range(count)])


def xor_sum(piece, axis, count):
    step = 1
    while step < count:
        piece = piece + lax.ppermute(piece, axis, [(d, d ^ step) for d in range(count)])
        step *= 2
    return piece


def body(block_input, tap_weight, mix_weight, head_grad):
    n_seq = lax.axis_size("seq")
    n_batch = lax.axis_size("batch")
    seqs, channels, t_local = block_input.shape
    local_channels = channels // n_seq
    hop = DILATION_STEP // t_local
    me = lax.axis_index("seq")
    kernel = lax.dynamic_slice_in_dim(tap_weight, me * local_channels, local_channels, axis=1).astype(jnp.float32)

    dy_blocks = head_grad.reshape(seqs, local_channels, n_seq, t_local).transpose(2, 0, 1, 3)

    first = exchange(jnp.stack([by_channel_block(block_input, n_seq), dy_blocks], axis=1))
    x_c = first[:, 0].astype(jnp.float32)
    upper = from_channel_blocks(first[:, 1])

    before_gelu = jnp.zeros(x_c.shape, jnp.float32)
    for k in range(TAPS):
        before_gelu = before_gelu + kernel[k][None, None, :, None] * shifted_blocks(x_c, (k - 4) * hop)
    activated, slope = gelu_parts(before_gelu)
    gated_c = activated.astype(jnp.bfloat16)

    backward = jnp.einsum("co,sot->sct", mix_weight, upper, preferred_element_type=jnp.float32)

    second = exchange(jnp.stack([gated_c, by_channel_block(backward.astype(jnp.bfloat16), n_seq)], axis=1))
    gated = from_channel_blocks(second[:, 0])
    backward_c = second[:, 1].astype(jnp.float32)

    mixed = jnp.einsum("co,sct->sot", mix_weight, gated, preferred_element_type=jnp.float32)
    block_output = (block_input.astype(jnp.float32) + mixed).astype(jnp.bfloat16)

    grad_pre = (backward_c * slope).astype(jnp.bfloat16).astype(jnp.float32)
    result = dy_blocks.astype(jnp.float32)
    for k in range(TAPS):
        result = result + kernel[k][None, None, :, None] * shifted_blocks(grad_pre, (4 - k) * hop)
    d_input = from_channel_blocks(exchange(result.astype(jnp.bfloat16)))

    local_taps = jnp.stack(
        [jnp.sum(grad_pre * shifted_blocks(x_c, (k - 4) * hop), axis=(0, 1, 3)) for k in range(TAPS)]
    )
    taps_all = xor_gather(xor_sum(local_taps, "batch", n_batch), "seq", n_seq)
    tap_grad = taps_all.transpose(1, 0, 2).reshape(TAPS, channels)

    part = local_channels // n_batch
    b = lax.axis_index("batch")
    both_gated = jnp.concatenate([gated] + [ring_shift(gated, "batch", n_batch, k) for k in range(1, n_batch)])
    both_upper = jnp.concatenate([upper] + [ring_shift(upper, "batch", n_batch, k) for k in range(1, n_batch)])
    all_seqs = both_gated.shape[0]
    picked = both_gated.reshape(all_seqs, n_seq, n_batch, part, t_local)
    picked = lax.dynamic_index_in_dim(picked, b, axis=2, keepdims=False)
    picked = picked.reshape(all_seqs, n_seq * part, t_local)
    partial_rows = lax.psum_scatter(
        jnp.einsum("sct,sot->co", picked, both_upper, preferred_element_type=jnp.float32),
        "seq",
        scatter_dimension=0,
        tiled=True,
    )
    mix_grad = xor_gather(partial_rows, "batch", n_batch).reshape(n_batch * part, channels)
    return (block_output, d_input, tap_grad, mix_grad)


def solution(mesh):
    placed = (P("batch", None, "seq"), P(), P(), P("batch", "seq", None))
    return jax.shard_map(
        body,
        mesh=mesh,
        in_specs=placed,
        out_specs=(P("batch", None, "seq"), P("batch", None, "seq"), P(), P("seq", None)),
        check_vma=False,
    )
```

```python
import math

import jax
import jax.numpy as jnp
from jax import lax
from jax.sharding import PartitionSpec as P

DILATION_STEP = 512
TAPS = 9


def gelu_parts(values):
    normal_cdf = 0.5 * (1.0 + jax.scipy.special.erf(values / math.sqrt(2.0)))
    normal_pdf = jnp.exp(-0.5 * values * values) / math.sqrt(2.0 * math.pi)
    return (values * normal_cdf, normal_cdf + values * normal_pdf)


def shifted_blocks(field, by):
    blocks = field.shape[0]
    if abs(by) >= blocks:
        return jnp.zeros_like(field)
    pad = [(0, 0)] * (field.ndim - 1)
    if by > 0:
        return jnp.pad(field[by:], [(0, by)] + pad)
    if by < 0:
        return jnp.pad(field[:by], [(-by, 0)] + pad)
    return field


def exchange(blocks):
    return lax.all_to_all(blocks, "seq", split_axis=0, concat_axis=0, tiled=True)


def by_channel_block(field, n):
    s, c, t = field.shape
    return field.reshape(s, n, c // n, t).transpose(1, 0, 2, 3)


def from_channel_blocks(blocks):
    n, s, cl, t = blocks.shape
    return blocks.transpose(1, 0, 2, 3).reshape(s, n * cl, t)


def xor_gather(piece, axis, count):
    me = lax.axis_index(axis)
    held = piece[None]
    step = 1
    while step < count:
        received = lax.ppermute(held, axis, [(d, d ^ step) for d in range(count)])
        low = ((me // step) % 2) == 0
        held = jnp.where(low, jnp.concatenate([held, received]), jnp.concatenate([received, held]))
        step *= 2
    return held


def ring_shift(piece, axis, count, by):
    return lax.ppermute(piece, axis, [(d, (d + by) % count) for d in range(count)])


def xor_sum(piece, axis, count):
    step = 1
    while step < count:
        piece = piece + lax.ppermute(piece, axis, [(d, d ^ step) for d in range(count)])
        step *= 2
    return piece


def body(block_input, tap_weight, mix_weight, head_grad):
    n_seq = lax.axis_size("seq")
    n_batch = lax.axis_size("batch")
    seqs, channels, t_local = block_input.shape
    local_channels = channels // n_seq
    hop = DILATION_STEP // t_local
    me = lax.axis_index("seq")
    kernel = lax.dynamic_slice_in_dim(tap_weight, me * local_channels, local_channels, axis=1).astype(jnp.float32)

    dy_blocks = head_grad.reshape(seqs, local_channels, n_seq, t_local).transpose(2, 0, 1, 3)

    first = exchange(jnp.stack([by_channel_block(block_input, n_seq), dy_blocks], axis=1))
    x_c = first[:, 0].astype(jnp.float32)
    upper = from_channel_blocks(first[:, 1])

    before_gelu = jnp.zeros(x_c.shape, jnp.float32)
    for k in range(TAPS):
        before_gelu = before_gelu + kernel[k][None, None, :, None] * shifted_blocks(x_c, (k - 4) * hop)
    activated, slope = gelu_parts(before_gelu)
    gated_c = activated.astype(jnp.bfloat16)

    backward = jnp.einsum("co,sot->sct", mix_weight, upper, preferred_element_type=jnp.float32)

    upper_others = [ring_shift(upper, "batch", n_batch, k) for k in range(1, n_batch)]
    second_in = jnp.stack([gated_c, by_channel_block(backward.astype(jnp.bfloat16), n_seq)], axis=1)
    upper_others, second_in = lax.optimization_barrier((upper_others, second_in))
    second = exchange(second_in)
    gated = from_channel_blocks(second[:, 0])
    backward_c = second[:, 1].astype(jnp.float32)

    mixed = jnp.einsum("co,sct->sot", mix_weight, gated, preferred_element_type=jnp.float32)
    block_output = (block_input.astype(jnp.float32) + mixed).astype(jnp.bfloat16)

    grad_pre = (backward_c * slope).astype(jnp.bfloat16).astype(jnp.float32)
    result = dy_blocks.astype(jnp.float32)
    for k in range(TAPS):
        result = result + kernel[k][None, None, :, None] * shifted_blocks(grad_pre, (4 - k) * hop)
    d_input = from_channel_blocks(exchange(result.astype(jnp.bfloat16)))

    local_taps = jnp.stack(
        [jnp.sum(grad_pre * shifted_blocks(x_c, (k - 4) * hop), axis=(0, 1, 3)) for k in range(TAPS)]
    )
    taps_all = xor_gather(xor_sum(local_taps, "batch", n_batch), "seq", n_seq)
    tap_grad = taps_all.transpose(1, 0, 2).reshape(TAPS, channels)

    part = local_channels // n_batch
    b = lax.axis_index("batch")
    rows_view = gated.reshape(seqs, n_seq, n_batch, part, t_local)
    own_rows = [lax.dynamic_index_in_dim(rows_view, b, axis=2, keepdims=False)]
    for k in range(1, n_batch):
        wanted = lax.dynamic_index_in_dim(rows_view, (b + k) % n_batch, axis=2, keepdims=False)
        own_rows.append(ring_shift(wanted, "batch", n_batch, k))
    picked = jnp.concatenate(own_rows).reshape(seqs * n_batch, n_seq * part, t_local)
    both_upper = jnp.concatenate([upper] + upper_others)
    partial_rows = lax.psum_scatter(
        jnp.einsum("sct,sot->co", picked, both_upper, preferred_element_type=jnp.float32),
        "seq",
        scatter_dimension=0,
        tiled=True,
    )
    mix_grad = xor_gather(partial_rows, "batch", n_batch).reshape(n_batch * part, channels)
    return (block_output, d_input, tap_grad, mix_grad)


def solution(mesh):
    placed = (P("batch", None, "seq"), P(), P(), P("batch", "seq", None))
    return jax.shard_map(
        body,
        mesh=mesh,
        in_specs=placed,
        out_specs=(P("batch", None, "seq"), P("batch", None, "seq"), P(), P("seq", None)),
        check_vma=False,
    )
```

```python
import math

import jax
import jax.numpy as jnp
from jax import lax
from jax.sharding import PartitionSpec as P

DILATION_STEP = 512
TAPS = 9


def gelu_parts(values):
    normal_cdf = 0.5 * (1.0 + jax.scipy.special.erf(values / math.sqrt(2.0)))
    normal_pdf = jnp.exp(-0.5 * values * values) / math.sqrt(2.0 * math.pi)
    return (values * normal_cdf, normal_cdf + values * normal_pdf)


def shifted_blocks(field, by):
    blocks = field.shape[0]
    if abs(by) >= blocks:
        return jnp.zeros_like(field)
    pad = [(0, 0)] * (field.ndim - 1)
    if by > 0:
        return jnp.pad(field[by:], [(0, by)] + pad)
    if by < 0:
        return jnp.pad(field[:by], [(-by, 0)] + pad)
    return field


def exchange(blocks):
    return lax.all_to_all(blocks, "seq", split_axis=0, concat_axis=0, tiled=True)


def by_channel_block(field, n):
    s, c, t = field.shape
    return field.reshape(s, n, c // n, t).transpose(1, 0, 2, 3)


def from_channel_blocks(blocks):
    n, s, cl, t = blocks.shape
    return blocks.transpose(1, 0, 2, 3).reshape(s, n * cl, t)


def xor_gather(piece, axis, count):
    me = lax.axis_index(axis)
    held = piece[None]
    step = 1
    while step < count:
        received = lax.ppermute(held, axis, [(d, d ^ step) for d in range(count)])
        low = ((me // step) % 2) == 0
        held = jnp.where(low, jnp.concatenate([held, received]), jnp.concatenate([received, held]))
        step *= 2
    return held


def ring_shift(piece, axis, count, by):
    return lax.ppermute(piece, axis, [(d, (d + by) % count) for d in range(count)])


def xor_sum(piece, axis, count):
    step = 1
    while step < count:
        piece = piece + lax.ppermute(piece, axis, [(d, d ^ step) for d in range(count)])
        step *= 2
    return piece


def body(block_input, tap_weight, mix_weight, head_grad):
    n_seq = lax.axis_size("seq")
    n_batch = lax.axis_size("batch")
    seqs, channels, t_local = block_input.shape
    local_channels = channels // n_seq
    hop = DILATION_STEP // t_local
    me = lax.axis_index("seq")
    kernel = lax.dynamic_slice_in_dim(tap_weight, me * local_channels, local_channels, axis=1).astype(jnp.float32)

    dy_blocks = head_grad.reshape(seqs, local_channels, n_seq, t_local).transpose(2, 0, 1, 3)

    first = exchange(jnp.stack([by_channel_block(block_input, n_seq), dy_blocks], axis=1))
    x_c = first[:, 0].astype(jnp.float32)
    upper = from_channel_blocks(first[:, 1])

    before_gelu = jnp.zeros(x_c.shape, jnp.float32)
    for k in range(TAPS):
        before_gelu = before_gelu + kernel[k][None, None, :, None] * shifted_blocks(x_c, (k - 4) * hop)
    activated, slope = gelu_parts(before_gelu)
    gated_c = activated.astype(jnp.bfloat16)

    backward = jnp.einsum("co,sot->sct", mix_weight, upper, preferred_element_type=jnp.float32)

    gated = from_channel_blocks(exchange(gated_c))
    upper_others = [ring_shift(upper, "batch", n_batch, k) for k in range(1, n_batch)]
    backward_send = by_channel_block(backward.astype(jnp.bfloat16), n_seq)
    gated, upper_others, backward_send = lax.optimization_barrier((gated, upper_others, backward_send))
    backward_c = exchange(backward_send).astype(jnp.float32)

    mixed = jnp.einsum("co,sct->sot", mix_weight, gated, preferred_element_type=jnp.float32)
    block_output = (block_input.astype(jnp.float32) + mixed).astype(jnp.bfloat16)

    grad_pre = (backward_c * slope).astype(jnp.bfloat16).astype(jnp.float32)
    result = dy_blocks.astype(jnp.float32)
    for k in range(TAPS):
        result = result + kernel[k][None, None, :, None] * shifted_blocks(grad_pre, (4 - k) * hop)
    d_input = from_channel_blocks(exchange(result.astype(jnp.bfloat16)))

    local_taps = jnp.stack(
        [jnp.sum(grad_pre * shifted_blocks(x_c, (k - 4) * hop), axis=(0, 1, 3)) for k in range(TAPS)]
    )
    taps_all = xor_gather(xor_sum(local_taps, "batch", n_batch), "seq", n_seq)
    tap_grad = taps_all.transpose(1, 0, 2).reshape(TAPS, channels)

    part = local_channels // n_batch
    b = lax.axis_index("batch")
    rows_view = gated.reshape(seqs, n_seq, n_batch, part, t_local)
    own_rows = [lax.dynamic_index_in_dim(rows_view, b, axis=2, keepdims=False)]
    for k in range(1, n_batch):
        wanted = lax.dynamic_index_in_dim(rows_view, (b + k) % n_batch, axis=2, keepdims=False)
        own_rows.append(ring_shift(wanted, "batch", n_batch, k))
    picked = jnp.concatenate(own_rows).reshape(seqs * n_batch, n_seq * part, t_local)
    both_upper = jnp.concatenate([upper] + upper_others)
    partial_rows = lax.psum_scatter(
        jnp.einsum("sct,sot->co", picked, both_upper, preferred_element_type=jnp.float32),
        "seq",
        scatter_dimension=0,
        tiled=True,
    )
    mix_grad = xor_gather(partial_rows, "batch", n_batch).reshape(n_batch * part, channels)
    return (block_output, d_input, tap_grad, mix_grad)


def solution(mesh):
    placed = (P("batch", None, "seq"), P(), P(), P("batch", "seq", None))
    return jax.shard_map(
        body,
        mesh=mesh,
        in_specs=placed,
        out_specs=(P("batch", None, "seq"), P("batch", None, "seq"), P(), P("seq", None)),
        check_vma=False,
    )
```

```python
import math

import jax
import jax.numpy as jnp
from jax import lax
from jax.sharding import PartitionSpec as P

DILATION_STEP = 512
TAPS = 9


def gelu_parts(values):
    normal_cdf = 0.5 * (1.0 + jax.scipy.special.erf(values / math.sqrt(2.0)))
    normal_pdf = jnp.exp(-0.5 * values * values) / math.sqrt(2.0 * math.pi)
    return (values * normal_cdf, normal_cdf + values * normal_pdf)


def shifted_blocks(field, by):
    blocks = field.shape[0]
    if abs(by) >= blocks:
        return jnp.zeros_like(field)
    pad = [(0, 0)] * (field.ndim - 1)
    if by > 0:
        return jnp.pad(field[by:], [(0, by)] + pad)
    if by < 0:
        return jnp.pad(field[:by], [(-by, 0)] + pad)
    return field


SEQ = ("seq_hi", "core")


def exchange(blocks):
    return lax.all_to_all(blocks, SEQ, split_axis=0, concat_axis=0, tiled=True)


def by_channel_block(field, n):
    s, c, t = field.shape
    return field.reshape(s, n, c // n, t).transpose(1, 0, 2, 3)


def from_channel_blocks(blocks):
    n, s, cl, t = blocks.shape
    return blocks.transpose(1, 0, 2, 3).reshape(s, n * cl, t)


def xor_gather(piece, axis, count, me):
    held = piece[None]
    step = 1
    while step < count:
        received = lax.ppermute(held, axis, [(d, d ^ step) for d in range(count)])
        low = ((me // step) % 2) == 0
        held = jnp.where(low, jnp.concatenate([held, received]), jnp.concatenate([received, held]))
        step *= 2
    return held


def ring_shift(piece, axis, count, by):
    return lax.ppermute(piece, axis, [(d, (d + by) % count) for d in range(count)])


def xor_sum(piece, axis, count):
    step = 1
    while step < count:
        piece = piece + lax.ppermute(piece, axis, [(d, d ^ step) for d in range(count)])
        step *= 2
    return piece


def body(block_input, tap_weight, mix_weight, head_grad):
    n_core = lax.axis_size("core")
    n_seq = lax.axis_size("seq_hi") * n_core
    n_batch = lax.axis_size("batch")
    seqs, channels, t_local = block_input.shape
    local_channels = channels // n_seq
    hop = DILATION_STEP // t_local
    c = lax.axis_index("core")
    b = lax.axis_index("batch")
    me = lax.axis_index("seq_hi") * n_core + c
    kernel = lax.dynamic_slice_in_dim(tap_weight, me * local_channels, local_channels, axis=1).astype(jnp.float32)

    dy_blocks = head_grad.reshape(seqs, local_channels, n_seq, t_local).transpose(2, 0, 1, 3)

    first = exchange(jnp.stack([by_channel_block(block_input, n_seq), dy_blocks], axis=1))
    x_c = first[:, 0].astype(jnp.float32)
    upper = from_channel_blocks(first[:, 1])

    before_gelu = jnp.zeros(x_c.shape, jnp.float32)
    for k in range(TAPS):
        before_gelu = before_gelu + kernel[k][None, None, :, None] * shifted_blocks(x_c, (k - 4) * hop)
    activated, slope = gelu_parts(before_gelu)
    gated_c = activated.astype(jnp.bfloat16)

    backward = jnp.einsum("co,sot->sct", mix_weight, upper, preferred_element_type=jnp.float32)

    gated = from_channel_blocks(exchange(gated_c))
    upper_others = [ring_shift(upper, "batch", n_batch, k) for k in range(1, n_batch)]
    backward_send = by_channel_block(backward.astype(jnp.bfloat16), n_seq)
    gated, upper_others, backward_send = lax.optimization_barrier((gated, upper_others, backward_send))
    backward_c = exchange(backward_send).astype(jnp.float32)

    mixed = jnp.einsum("co,sct->sot", mix_weight, gated, preferred_element_type=jnp.float32)
    block_output = (block_input.astype(jnp.float32) + mixed).astype(jnp.bfloat16)

    grad_pre = (backward_c * slope).astype(jnp.bfloat16).astype(jnp.float32)
    result = dy_blocks.astype(jnp.float32)
    for k in range(TAPS):
        result = result + kernel[k][None, None, :, None] * shifted_blocks(grad_pre, (4 - k) * hop)
    d_input = from_channel_blocks(exchange(result.astype(jnp.bfloat16)))

    local_taps = jnp.stack(
        [jnp.sum(grad_pre * shifted_blocks(x_c, (k - 4) * hop), axis=(0, 1, 3)) for k in range(TAPS)]
    )
    taps_all = xor_gather(xor_sum(local_taps, "batch", n_batch), SEQ, n_seq, me)
    tap_grad = taps_all.transpose(1, 0, 2).reshape(TAPS, channels)

    quarter = local_channels // (n_batch * n_core)
    rows_view = gated.reshape(seqs, n_seq, n_batch, n_core * quarter, t_local)
    batch_rows = [lax.dynamic_index_in_dim(rows_view, b, axis=2, keepdims=False)]
    for k in range(1, n_batch):
        wanted = lax.dynamic_index_in_dim(rows_view, (b + k) % n_batch, axis=2, keepdims=False)
        batch_rows.append(ring_shift(wanted, "batch", n_batch, k))
    batch_rows = jnp.concatenate(batch_rows).reshape(seqs * n_batch, n_seq, n_core, quarter, t_local)
    batch_upper = jnp.concatenate([upper] + upper_others)
    picked = jnp.concatenate([
        lax.dynamic_index_in_dim(batch_rows, c, axis=2, keepdims=False),
        ring_shift(lax.dynamic_index_in_dim(batch_rows, 1 - c, axis=2, keepdims=False), "core", n_core, 1),
    ]).reshape(seqs * n_batch * n_core, n_seq * quarter, t_local)
    both_upper = jnp.concatenate([batch_upper, ring_shift(batch_upper, "core", n_core, 1)])
    partial_rows = lax.psum_scatter(
        jnp.einsum("sct,sot->co", picked, both_upper, preferred_element_type=jnp.float32),
        "seq_hi",
        scatter_dimension=0,
        tiled=True,
    ).reshape(n_core, quarter, channels)
    mine = lax.dynamic_index_in_dim(partial_rows, c, axis=0, keepdims=False)
    theirs = ring_shift(lax.dynamic_index_in_dim(partial_rows, 1 - c, axis=0, keepdims=False), "core", n_core, 1)
    halves = jnp.where(c == 0, jnp.concatenate([mine, theirs]), jnp.concatenate([theirs, mine]))
    mix_grad = xor_gather(halves, "batch", n_batch, b).reshape(n_batch * n_core * quarter, channels)
    return (block_output, d_input, tap_grad, mix_grad)


def solution(mesh):
    devices = mesh.devices
    inner = jax.sharding.Mesh(devices.reshape(devices.shape[0] // 2, 2, devices.shape[1]), ("seq_hi", "core", "batch"))
    placed = (P("batch", None, SEQ), P(), P(), P("batch", SEQ, None))
    return jax.shard_map(
        body,
        mesh=inner,
        in_specs=placed,
        out_specs=(P("batch", None, SEQ), P("batch", None, SEQ), P(), P(SEQ, None)),
        check_vma=False,
    )
```

```python
import math

import jax
import jax.numpy as jnp
from jax import lax
from jax.sharding import PartitionSpec as P

DILATION_STEP = 512
TAPS = 9


def gelu_parts(values):
    normal_cdf = 0.5 * (1.0 + jax.scipy.special.erf(values / math.sqrt(2.0)))
    normal_pdf = jnp.exp(-0.5 * values * values) / math.sqrt(2.0 * math.pi)
    return (values * normal_cdf, normal_cdf + values * normal_pdf)


def shifted_blocks(field, by):
    blocks = field.shape[0]
    if abs(by) >= blocks:
        return jnp.zeros_like(field)
    pad = [(0, 0)] * (field.ndim - 1)
    if by > 0:
        return jnp.pad(field[by:], [(0, by)] + pad)
    if by < 0:
        return jnp.pad(field[:by], [(-by, 0)] + pad)
    return field


def exchange(blocks):
    return lax.all_to_all(blocks, "seq", split_axis=0, concat_axis=0, tiled=True)


def by_channel_block(field, n):
    s, c, t = field.shape
    return field.reshape(s, n, c // n, t).transpose(1, 0, 2, 3)


def from_channel_blocks(blocks):
    n, s, cl, t = blocks.shape
    return blocks.transpose(1, 0, 2, 3).reshape(s, n * cl, t)


def xor_gather(piece, axis, count):
    me = lax.axis_index(axis)
    held = piece[None]
    step = 1
    while step < count:
        received = lax.ppermute(held, axis, [(d, d ^ step) for d in range(count)])
        low = ((me // step) % 2) == 0
        held = jnp.where(low, jnp.concatenate([held, received]), jnp.concatenate([received, held]))
        step *= 2
    return held


def ring_shift(piece, axis, count, by):
    return lax.ppermute(piece, axis, [(d, (d + by) % count) for d in range(count)])


def xor_sum(piece, axis, count):
    step = 1
    while step < count:
        piece = piece + lax.ppermute(piece, axis, [(d, d ^ step) for d in range(count)])
        step *= 2
    return piece


def body(block_input, tap_weight, mix_weight, head_grad):
    n_seq = lax.axis_size("seq")
    n_batch = lax.axis_size("batch")
    seqs, channels, t_local = block_input.shape
    local_channels = channels // n_seq
    hop = DILATION_STEP // t_local
    me = lax.axis_index("seq")
    kernel = lax.dynamic_slice_in_dim(tap_weight, me * local_channels, local_channels, axis=1).astype(jnp.float32)

    dy_blocks = head_grad.reshape(seqs, local_channels, n_seq, t_local).transpose(2, 0, 1, 3)

    x_recv = exchange(by_channel_block(block_input, n_seq))
    x_recv, dy_send = lax.optimization_barrier((x_recv, dy_blocks))
    x_c = x_recv.astype(jnp.float32)
    upper = from_channel_blocks(exchange(dy_send))

    before_gelu = jnp.zeros(x_c.shape, jnp.float32)
    for k in range(TAPS):
        before_gelu = before_gelu + kernel[k][None, None, :, None] * shifted_blocks(x_c, (k - 4) * hop)
    activated, slope = gelu_parts(before_gelu)
    gated_c = activated.astype(jnp.bfloat16)

    backward = jnp.einsum("co,sot->sct", mix_weight, upper, preferred_element_type=jnp.float32)

    gated = from_channel_blocks(exchange(gated_c))
    upper_others = [ring_shift(upper, "batch", n_batch, k) for k in range(1, n_batch)]
    backward_send = by_channel_block(backward.astype(jnp.bfloat16), n_seq)
    gated, upper_others, backward_send = lax.optimization_barrier((gated, upper_others, backward_send))
    backward_c = exchange(backward_send).astype(jnp.float32)

    mixed = jnp.einsum("co,sct->sot", mix_weight, gated, preferred_element_type=jnp.float32)
    block_output = (block_input.astype(jnp.float32) + mixed).astype(jnp.bfloat16)

    grad_pre = (backward_c * slope).astype(jnp.bfloat16).astype(jnp.float32)
    result = dy_blocks.astype(jnp.float32)
    for k in range(TAPS):
        result = result + kernel[k][None, None, :, None] * shifted_blocks(grad_pre, (4 - k) * hop)
    d_send, block_output = lax.optimization_barrier((result.astype(jnp.bfloat16), block_output))
    d_input = from_channel_blocks(exchange(d_send))

    local_taps = jnp.stack(
        [jnp.sum(grad_pre * shifted_blocks(x_c, (k - 4) * hop), axis=(0, 1, 3)) for k in range(TAPS)]
    )
    taps_all = xor_gather(xor_sum(local_taps, "batch", n_batch), "seq", n_seq)
    tap_grad = taps_all.transpose(1, 0, 2).reshape(TAPS, channels)

    part = local_channels // n_batch
    b = lax.axis_index("batch")
    rows_view = gated.reshape(seqs, n_seq, n_batch, part, t_local)
    own_rows = [lax.dynamic_index_in_dim(rows_view, b, axis=2, keepdims=False)]
    for k in range(1, n_batch):
        wanted = lax.dynamic_index_in_dim(rows_view, (b + k) % n_batch, axis=2, keepdims=False)
        own_rows.append(ring_shift(wanted, "batch", n_batch, k))
    picked = jnp.concatenate(own_rows).reshape(seqs * n_batch, n_seq * part, t_local)
    both_upper = jnp.concatenate([upper] + upper_others)
    partial_rows = lax.psum_scatter(
        jnp.einsum("sct,sot->co", picked, both_upper, preferred_element_type=jnp.float32),
        "seq",
        scatter_dimension=0,
        tiled=True,
    )
    mix_grad = xor_gather(partial_rows, "batch", n_batch).reshape(n_batch * part, channels)
    return (block_output, d_input, tap_grad, mix_grad)


def solution(mesh):
    placed = (P("batch", None, "seq"), P(), P(), P("batch", "seq", None))
    return jax.shard_map(
        body,
        mesh=mesh,
        in_specs=placed,
        out_specs=(P("batch", None, "seq"), P("batch", None, "seq"), P(), P("seq", None)),
        check_vma=False,
    )
```

```python
import math

import jax
import jax.numpy as jnp
from jax import lax
from jax.sharding import PartitionSpec as P

DILATION_STEP = 512
TAPS = 9


def gelu_parts(values):
    normal_cdf = 0.5 * (1.0 + jax.scipy.special.erf(values / math.sqrt(2.0)))
    normal_pdf = jnp.exp(-0.5 * values * values) / math.sqrt(2.0 * math.pi)
    return (values * normal_cdf, normal_cdf + values * normal_pdf)


def shifted_blocks(field, by):
    blocks = field.shape[0]
    if abs(by) >= blocks:
        return jnp.zeros_like(field)
    pad = [(0, 0)] * (field.ndim - 1)
    if by > 0:
        return jnp.pad(field[by:], [(0, by)] + pad)
    if by < 0:
        return jnp.pad(field[:by], [(-by, 0)] + pad)
    return field


def exchange(blocks):
    return lax.all_to_all(blocks, "seq", split_axis=0, concat_axis=0, tiled=True)


def by_channel_block(field, n):
    s, c, t = field.shape
    return field.reshape(s, n, c // n, t).transpose(1, 0, 2, 3)


def from_channel_blocks(blocks):
    n, s, cl, t = blocks.shape
    return blocks.transpose(1, 0, 2, 3).reshape(s, n * cl, t)


def xor_gather(piece, axis, count):
    me = lax.axis_index(axis)
    held = piece[None]
    step = 1
    while step < count:
        received = lax.ppermute(held, axis, [(d, d ^ step) for d in range(count)])
        low = ((me // step) % 2) == 0
        held = jnp.where(low, jnp.concatenate([held, received]), jnp.concatenate([received, held]))
        step *= 2
    return held


def ring_shift(piece, axis, count, by):
    return lax.ppermute(piece, axis, [(d, (d + by) % count) for d in range(count)])


def halving_scatter(whole, axis, count, me):
    bits = count.bit_length() - 1
    rows = whole.shape[0] // count
    held = whole.reshape((2,) * bits + (rows,) + whole.shape[1:])
    for bit in range(bits):
        mask = 1 << bit
        side = (me // mask) % 2
        keep = lax.dynamic_index_in_dim(held, side, axis=bits - 1 - bit, keepdims=False)
        send = lax.dynamic_index_in_dim(held, 1 - side, axis=bits - 1 - bit, keepdims=False)
        held = keep + lax.ppermute(send, axis, [(d, d ^ mask) for d in range(count)])
    return held


def xor_sum(piece, axis, count):
    step = 1
    while step < count:
        piece = piece + lax.ppermute(piece, axis, [(d, d ^ step) for d in range(count)])
        step *= 2
    return piece


def body(block_input, tap_weight, mix_weight, head_grad):
    n_seq = lax.axis_size("seq")
    n_batch = lax.axis_size("batch")
    seqs, channels, t_local = block_input.shape
    local_channels = channels // n_seq
    hop = DILATION_STEP // t_local
    me = lax.axis_index("seq")
    kernel = lax.dynamic_slice_in_dim(tap_weight, me * local_channels, local_channels, axis=1).astype(jnp.float32)

    dy_blocks = head_grad.reshape(seqs, local_channels, n_seq, t_local).transpose(2, 0, 1, 3)

    first = exchange(jnp.stack([by_channel_block(block_input, n_seq), dy_blocks], axis=1))
    x_c = first[:, 0].astype(jnp.float32)
    upper = from_channel_blocks(first[:, 1])

    before_gelu = jnp.zeros(x_c.shape, jnp.float32)
    for k in range(TAPS):
        before_gelu = before_gelu + kernel[k][None, None, :, None] * shifted_blocks(x_c, (k - 4) * hop)
    activated, slope = gelu_parts(before_gelu)
    gated_c = activated.astype(jnp.bfloat16)

    backward = jnp.einsum("co,sot->sct", mix_weight, upper, preferred_element_type=jnp.float32)

    gated = from_channel_blocks(exchange(gated_c))
    upper_others = [ring_shift(upper, "batch", n_batch, k) for k in range(1, n_batch)]
    backward_send = by_channel_block(backward.astype(jnp.bfloat16), n_seq)
    gated, upper_others, backward_send = lax.optimization_barrier((gated, upper_others, backward_send))
    backward_c = exchange(backward_send).astype(jnp.float32)

    mixed = jnp.einsum("co,sct->sot", mix_weight, gated, preferred_element_type=jnp.float32)
    block_output = (block_input.astype(jnp.float32) + mixed).astype(jnp.bfloat16)

    grad_pre = (backward_c * slope).astype(jnp.bfloat16).astype(jnp.float32)
    result = dy_blocks.astype(jnp.float32)
    for k in range(TAPS):
        result = result + kernel[k][None, None, :, None] * shifted_blocks(grad_pre, (4 - k) * hop)
    d_input = from_channel_blocks(exchange(result.astype(jnp.bfloat16)))

    local_taps = jnp.stack(
        [jnp.sum(grad_pre * shifted_blocks(x_c, (k - 4) * hop), axis=(0, 1, 3)) for k in range(TAPS)]
    )
    taps_all = xor_gather(xor_sum(local_taps, "batch", n_batch), "seq", n_seq)
    tap_grad = taps_all.transpose(1, 0, 2).reshape(TAPS, channels)

    part = local_channels // n_batch
    b = lax.axis_index("batch")
    rows_view = gated.reshape(seqs, n_seq, n_batch, part, t_local)
    own_rows = [lax.dynamic_index_in_dim(rows_view, b, axis=2, keepdims=False)]
    for k in range(1, n_batch):
        wanted = lax.dynamic_index_in_dim(rows_view, (b + k) % n_batch, axis=2, keepdims=False)
        own_rows.append(ring_shift(wanted, "batch", n_batch, k))
    picked = jnp.concatenate(own_rows).reshape(seqs * n_batch, n_seq * part, t_local)
    both_upper = jnp.concatenate([upper] + upper_others)
    partial_rows = halving_scatter(
        jnp.einsum("sct,sot->co", picked, both_upper, preferred_element_type=jnp.float32), "seq", n_seq, me
    )
    mix_grad = xor_gather(partial_rows, "batch", n_batch).reshape(n_batch * part, channels)
    return (block_output, d_input, tap_grad, mix_grad)


def solution(mesh):
    placed = (P("batch", None, "seq"), P(), P(), P("batch", "seq", None))
    return jax.shard_map(
        body,
        mesh=mesh,
        in_specs=placed,
        out_specs=(P("batch", None, "seq"), P("batch", None, "seq"), P(), P("seq", None)),
        check_vma=False,
    )
```

```python
import math

import jax
import jax.numpy as jnp
from jax import lax
from jax.sharding import PartitionSpec as P

DILATION_STEP = 512
TAPS = 9


def gelu_parts(values):
    normal_cdf = 0.5 * (1.0 + jax.scipy.special.erf(values / math.sqrt(2.0)))
    normal_pdf = jnp.exp(-0.5 * values * values) / math.sqrt(2.0 * math.pi)
    return (values * normal_cdf, normal_cdf + values * normal_pdf)


def shifted_blocks(field, by):
    blocks = field.shape[0]
    if abs(by) >= blocks:
        return jnp.zeros_like(field)
    pad = [(0, 0)] * (field.ndim - 1)
    if by > 0:
        return jnp.pad(field[by:], [(0, by)] + pad)
    if by < 0:
        return jnp.pad(field[:by], [(-by, 0)] + pad)
    return field


def exchange(blocks):
    return lax.all_to_all(blocks, "seq", split_axis=0, concat_axis=0, tiled=True)


def by_channel_block(field, n):
    s, c, t = field.shape
    return field.reshape(s, n, c // n, t).transpose(1, 0, 2, 3)


def from_channel_blocks(blocks):
    n, s, cl, t = blocks.shape
    return blocks.transpose(1, 0, 2, 3).reshape(s, n * cl, t)


def xor_gather(piece, axis, count):
    me = lax.axis_index(axis)
    held = piece[None]
    step = 1
    while step < count:
        received = lax.ppermute(held, axis, [(d, d ^ step) for d in range(count)])
        low = ((me // step) % 2) == 0
        held = jnp.where(low, jnp.concatenate([held, received]), jnp.concatenate([received, held]))
        step *= 2
    return held


def ring_shift(piece, axis, count, by):
    return lax.ppermute(piece, axis, [(d, (d + by) % count) for d in range(count)])


def halving_scatter(whole, axis, count, me):
    bits = count.bit_length() - 1
    rows = whole.shape[0] // count
    held = whole.reshape((2,) * bits + (rows,) + whole.shape[1:])
    for bit in range(bits):
        mask = 1 << bit
        side = (me // mask) % 2
        keep = lax.dynamic_index_in_dim(held, side, axis=bits - 1 - bit, keepdims=False)
        send = lax.dynamic_index_in_dim(held, 1 - side, axis=bits - 1 - bit, keepdims=False)
        held = keep + lax.ppermute(send, axis, [(d, d ^ mask) for d in range(count)])
    return held


def xor_sum(piece, axis, count):
    step = 1
    while step < count:
        piece = piece + lax.ppermute(piece, axis, [(d, d ^ step) for d in range(count)])
        step *= 2
    return piece


def body(block_input, tap_weight, mix_weight, head_grad):
    n_seq = lax.axis_size("seq")
    n_batch = lax.axis_size("batch")
    seqs, channels, t_local = block_input.shape
    local_channels = channels // n_seq
    hop = DILATION_STEP // t_local
    me = lax.axis_index("seq")
    kernel = lax.dynamic_slice_in_dim(tap_weight, me * local_channels, local_channels, axis=1).astype(jnp.float32)

    dy_blocks = head_grad.reshape(seqs, local_channels, n_seq, t_local).transpose(2, 0, 1, 3)

    first = exchange(jnp.stack([by_channel_block(block_input, n_seq), dy_blocks], axis=1))
    x_c = first[:, 0].astype(jnp.float32)
    upper = from_channel_blocks(first[:, 1])

    before_gelu = jnp.zeros(x_c.shape, jnp.float32)
    for k in range(TAPS):
        before_gelu = before_gelu + kernel[k][None, None, :, None] * shifted_blocks(x_c, (k - 4) * hop)
    activated, slope = gelu_parts(before_gelu)
    gated_c = activated.astype(jnp.bfloat16)

    backward = jnp.einsum("co,sot->sct", mix_weight, upper, preferred_element_type=jnp.float32)

    gated = from_channel_blocks(exchange(gated_c))
    upper_others = [ring_shift(upper, "batch", n_batch, k) for k in range(1, n_batch)]
    backward_send = by_channel_block(backward.astype(jnp.bfloat16), n_seq)
    gated, upper_others, backward_send = lax.optimization_barrier((gated, upper_others, backward_send))
    backward_c = exchange(backward_send).astype(jnp.float32)

    mixed = jnp.einsum("co,sct->sot", mix_weight, gated, preferred_element_type=jnp.float32)
    block_output = (block_input.astype(jnp.float32) + mixed).astype(jnp.bfloat16)

    grad_pre = (backward_c * slope).astype(jnp.bfloat16).astype(jnp.float32)
    result = dy_blocks.astype(jnp.float32)
    for k in range(TAPS):
        result = result + kernel[k][None, None, :, None] * shifted_blocks(grad_pre, (4 - k) * hop)
    d_send, block_output = lax.optimization_barrier((result.astype(jnp.bfloat16), block_output))
    d_input = from_channel_blocks(exchange(d_send))

    local_taps = jnp.stack(
        [jnp.sum(grad_pre * shifted_blocks(x_c, (k - 4) * hop), axis=(0, 1, 3)) for k in range(TAPS)]
    )
    taps_all = xor_gather(xor_sum(local_taps, "batch", n_batch), "seq", n_seq)
    tap_grad = taps_all.transpose(1, 0, 2).reshape(TAPS, channels)

    part = local_channels // n_batch
    b = lax.axis_index("batch")
    rows_view = gated.reshape(seqs, n_seq, n_batch, part, t_local)
    own_rows = [lax.dynamic_index_in_dim(rows_view, b, axis=2, keepdims=False)]
    for k in range(1, n_batch):
        wanted = lax.dynamic_index_in_dim(rows_view, (b + k) % n_batch, axis=2, keepdims=False)
        own_rows.append(ring_shift(wanted, "batch", n_batch, k))
    picked = jnp.concatenate(own_rows).reshape(seqs * n_batch, n_seq * part, t_local)
    both_upper = jnp.concatenate([upper] + upper_others)
    partial_rows = halving_scatter(
        jnp.einsum("sct,sot->co", picked, both_upper, preferred_element_type=jnp.float32), "seq", n_seq, me
    )
    mix_grad = xor_gather(partial_rows, "batch", n_batch).reshape(n_batch * part, channels)
    return (block_output, d_input, tap_grad, mix_grad)


def solution(mesh):
    placed = (P("batch", None, "seq"), P(), P(), P("batch", "seq", None))
    return jax.shard_map(
        body,
        mesh=mesh,
        in_specs=placed,
        out_specs=(P("batch", None, "seq"), P("batch", None, "seq"), P(), P("seq", None)),
        check_vma=False,
    )
```

```python
import math

import jax
import jax.numpy as jnp
from jax import lax
from jax.sharding import PartitionSpec as P

DILATION_STEP = 512
TAPS = 9


def gelu_parts(values):
    normal_cdf = 0.5 * (1.0 + jax.scipy.special.erf(values / math.sqrt(2.0)))
    normal_pdf = jnp.exp(-0.5 * values * values) / math.sqrt(2.0 * math.pi)
    return (values * normal_cdf, normal_cdf + values * normal_pdf)


def shifted_blocks(field, by):
    blocks = field.shape[0]
    if abs(by) >= blocks:
        return jnp.zeros_like(field)
    pad = [(0, 0)] * (field.ndim - 1)
    if by > 0:
        return jnp.pad(field[by:], [(0, by)] + pad)
    if by < 0:
        return jnp.pad(field[:by], [(-by, 0)] + pad)
    return field


def exchange(blocks):
    return lax.all_to_all(blocks, "seq", split_axis=0, concat_axis=0, tiled=True)


def by_channel_block(field, n):
    s, c, t = field.shape
    return field.reshape(s, n, c // n, t).transpose(1, 0, 2, 3)


def from_channel_blocks(blocks):
    n, s, cl, t = blocks.shape
    return blocks.transpose(1, 0, 2, 3).reshape(s, n * cl, t)


def xor_gather(piece, axis, count):
    me = lax.axis_index(axis)
    held = piece[None]
    step = 1
    while step < count:
        received = lax.ppermute(held, axis, [(d, d ^ step) for d in range(count)])
        low = ((me // step) % 2) == 0
        held = jnp.where(low, jnp.concatenate([held, received]), jnp.concatenate([received, held]))
        step *= 2
    return held


def ring_shift(piece, axis, count, by):
    return lax.ppermute(piece, axis, [(d, (d + by) % count) for d in range(count)])


def halving_scatter(whole, axis, count, me):
    bits = count.bit_length() - 1
    rows = whole.shape[0] // count
    held = whole.reshape((2,) * bits + (rows,) + whole.shape[1:])
    for bit in range(bits):
        mask = 1 << bit
        side = (me // mask) % 2
        keep = lax.dynamic_index_in_dim(held, side, axis=bits - 1 - bit, keepdims=False)
        send = lax.dynamic_index_in_dim(held, 1 - side, axis=bits - 1 - bit, keepdims=False)
        held = keep + lax.ppermute(send, axis, [(d, d ^ mask) for d in range(count)])
    return held


def xor_sum(piece, axis, count):
    step = 1
    while step < count:
        piece = piece + lax.ppermute(piece, axis, [(d, d ^ step) for d in range(count)])
        step *= 2
    return piece


def body(block_input, tap_weight, mix_weight, head_grad):
    n_seq = lax.axis_size("seq")
    n_batch = lax.axis_size("batch")
    seqs, channels, t_local = block_input.shape
    local_channels = channels // n_seq
    hop = DILATION_STEP // t_local
    me = lax.axis_index("seq")
    kernel = lax.dynamic_slice_in_dim(tap_weight, me * local_channels, local_channels, axis=1).astype(jnp.float32)

    dy_blocks = head_grad.reshape(seqs, local_channels, n_seq, t_local).transpose(2, 0, 1, 3)

    first = exchange(jnp.stack([by_channel_block(block_input, n_seq), dy_blocks], axis=1))
    x_c = first[:, 0].astype(jnp.float32)
    upper = from_channel_blocks(first[:, 1])

    before_gelu = jnp.zeros(x_c.shape, jnp.float32)
    for k in range(TAPS):
        before_gelu = before_gelu + kernel[k][None, None, :, None] * shifted_blocks(x_c, (k - 4) * hop)
    activated, slope = gelu_parts(before_gelu)
    gated_c = activated.astype(jnp.bfloat16)

    backward = jnp.einsum("co,sot->sct", mix_weight, upper, preferred_element_type=jnp.float32)

    upper_others = [ring_shift(upper, "batch", n_batch, k) for k in range(1, n_batch)]
    second_in = jnp.stack([gated_c, by_channel_block(backward.astype(jnp.bfloat16), n_seq)], axis=1)
    upper_others, second_in = lax.optimization_barrier((upper_others, second_in))
    second = exchange(second_in)
    gated = from_channel_blocks(second[:, 0])
    backward_c = second[:, 1].astype(jnp.float32)

    mixed = jnp.einsum("co,sct->sot", mix_weight, gated, preferred_element_type=jnp.float32)
    block_output = (block_input.astype(jnp.float32) + mixed).astype(jnp.bfloat16)

    grad_pre = (backward_c * slope).astype(jnp.bfloat16).astype(jnp.float32)
    result = dy_blocks.astype(jnp.float32)
    for k in range(TAPS):
        result = result + kernel[k][None, None, :, None] * shifted_blocks(grad_pre, (4 - k) * hop)
    d_input = from_channel_blocks(exchange(result.astype(jnp.bfloat16)))

    local_taps = jnp.stack(
        [jnp.sum(grad_pre * shifted_blocks(x_c, (k - 4) * hop), axis=(0, 1, 3)) for k in range(TAPS)]
    )
    taps_all = xor_gather(xor_sum(local_taps, "batch", n_batch), "seq", n_seq)
    tap_grad = taps_all.transpose(1, 0, 2).reshape(TAPS, channels)

    part = local_channels // n_batch
    b = lax.axis_index("batch")
    rows_view = gated.reshape(seqs, n_seq, n_batch, part, t_local)
    own_rows = [lax.dynamic_index_in_dim(rows_view, b, axis=2, keepdims=False)]
    for k in range(1, n_batch):
        wanted = lax.dynamic_index_in_dim(rows_view, (b + k) % n_batch, axis=2, keepdims=False)
        own_rows.append(ring_shift(wanted, "batch", n_batch, k))
    picked = jnp.concatenate(own_rows).reshape(seqs * n_batch, n_seq * part, t_local)
    both_upper = jnp.concatenate([upper] + upper_others)
    partial_rows = halving_scatter(
        jnp.einsum("sct,sot->co", picked, both_upper, preferred_element_type=jnp.float32), "seq", n_seq, me
    )
    mix_grad = xor_gather(partial_rows, "batch", n_batch).reshape(n_batch * part, channels)
    return (block_output, d_input, tap_grad, mix_grad)


def solution(mesh):
    placed = (P("batch", None, "seq"), P(), P(), P("batch", "seq", None))
    return jax.shard_map(
        body,
        mesh=mesh,
        in_specs=placed,
        out_specs=(P("batch", None, "seq"), P("batch", None, "seq"), P(), P("seq", None)),
        check_vma=False,
    )
```
